32 devices in a mesh: groups: 2 (over y), row: 16 (over z, x, core).
Axes of the slice: x: 2, y: 2, z: 4, core: 2. Of those that a mesh axis runs over, the one named last changes fastest.
Arguments:
- features: bfloat16 [576, 16384], P(None, ('groups', 'row')), parts along dimension 1, may hold values from -150 to 150
- labels: int32 [16384], P(('groups', 'row')), parts along dimension 0, may hold values 0 or 1
- other_predictor: float32 [16384], P(('groups', 'row')), parts along dimension 0, may hold values from -6 to 6
- coefficients: float32 [8192], P('groups'), parts along dimension 0, may hold values from -0.09375 to 0.09375
- panel_block: int32 [2], P('groups'), parts along dimension 0, may hold values from 0 to 55
Outputs:
- r_factor: float32 [1152, 576], P('groups'), parts along dimension 0
- residual: float32 [16384], P(('groups', 'row')), parts along dimension 0
The draws below stay inside these ranges and needn't reach their ends.
There are 2 independent parts, one for each index of `groups`. The reference program is written for one: setup_inputs(seed, part) draws one part's arguments, and reference() takes and returns one part's arrays. A program takes and returns all parts, laid end to end along the dimension named above; each array names one. Nothing has to cross between parts.
All inputs are finite; a program needn't handle non-finite values. No bound on the sum of `labels` on one device may be relied on, other than what follows from the above.
Results may differ from the reference program's by a relative error of at most 0.0003.
Values sent between devices are 32-bit elements; how exact they have to be, the bound alone decides.
No kernel may reach another device: no remote copies, remote signals or barrier semaphores. Data moves between devices by JAX's collectives and lax.ppermute only.
A program may use at most 64 MiB of HBM per device.

```python
import math
import jax
import jax.numpy as jnp
from jax import lax

FEAT = 4096
WIN = 576
PB = 64
NPAN = 9
ROWS = 8192


def draw_features(key, part):
    subkeys = jax.random.split(key, 5)
    noise_draw = jax.random.truncated_normal(subkeys[0], -4.0, 4.0, (WIN + 2, ROWS), jnp.float32)
    common = jax.random.truncated_normal(subkeys[1], -4.0, 4.0, (ROWS,), jnp.float32)
    loading = jax.random.uniform(subkeys[3], (WIN,), jnp.float32, -1.0, 1.0)
    column_scale = jnp.exp(jax.random.uniform(subkeys[4], (WIN,), jnp.float32, math.log(0.5), math.log(5.0)))
    drift_row = jnp.exp(0.5 * math.log(3.0) * jnp.arange(ROWS, dtype=jnp.float32) / ROWS)
    mixed = noise_draw[2:] + 0.5 * noise_draw[1:-1] + 0.3 * noise_draw[:-2] + 0.6 * loading[:, None] * common[None, :]
    return (mixed * column_scale[:, None] * drift_row[None, :]).astype(jnp.bfloat16)


def touch_ends(entries, rng, low, largest):
    shape = entries.shape
    spot = [jax.random.randint(jax.random.fold_in(rng, axis), (), 0, shape[axis]) for axis in range(len(shape))]
    entries = entries.at[tuple(spot)].set(low)
    longest = shape.index(max(shape))
    spot[longest] = (spot[longest] + 1) % shape[longest]
    return entries.at[tuple(spot)].set(largest)


def steps_of(rng, shape, pieces, least, high):
    loudness = 1.0
    for position, parts in pieces:
        heights = jax.random.uniform(jax.random.fold_in(jax.random.fold_in(rng, 6), position), (parts,), jnp.float32, least / len(pieces), high / len(pieces))
        loudness = loudness * jnp.repeat(jnp.exp(heights), shape[position] // parts).reshape((-1,) + (1,) * (len(shape) - 1 - position))
    return loudness


def gaussian(rng, dims, width, limit, shards=(), kind=jnp.bfloat16):
    level = steps_of(rng, dims, shards, -0.22, 0.18) if shards else 1.0
    drawn = jax.random.normal(rng, dims, jnp.float32) * width * level
    return jnp.minimum(jnp.maximum(drawn, -limit), limit).astype(kind)


def setup_inputs(seed: int = 0, part: int = 0) -> dict:
    keys = jax.random.split(jax.random.key(seed), 6)
    part_keys = jax.random.split(jax.random.fold_in(keys[5], part), 6)
    return {
        "features": draw_features(jax.random.fold_in(jax.random.fold_in(keys[5], part), 71), part),
        "labels": touch_ends((jax.random.randint(part_keys[1], (ROWS,), 0, 2) < 1).astype(jnp.int32), jax.random.fold_in(part_keys[1], 1), 0, 1),
        "other_predictor": gaussian(part_keys[2], (ROWS,), 1.0, 6.0, ((0, 16),), jnp.float32),
        "coefficients": gaussian(part_keys[3], (FEAT,), (8 * WIN) ** -0.5, 0.09375, (), jnp.float32),
        "panel_block": jax.random.randint(part_keys[4], (1,), 0, (FEAT - WIN) // PB + 1).astype(jnp.int32),
    }


precise = lax.Precision.HIGHEST

def inner_rows(left_rows, right_rows):
    return lax.dot_general(left_rows, right_rows, (((1,), (1,)), ((), ())), precision=precise)

def reference(features, labels, other_predictor, coefficients, panel_block):
    first_col = (panel_block[0] * PB).astype(jnp.int32)
    window_coef = lax.dynamic_slice(coefficients, (first_col,), (WIN,))
    as_float = features.astype(jnp.float32)
    linear = jnp.dot(window_coef, as_float, precision=precise) + other_predictor
    fitted = jax.nn.sigmoid(linear)
    weight = jnp.maximum(fitted * (1.0 - fitted), 0.01)
    root_weight = jnp.sqrt(weight)
    norm_scale = 1.0 / math.sqrt(ROWS)
    scaled = as_float * (root_weight * norm_scale)[None, :]
    target = (root_weight * linear + (labels.astype(jnp.float32) - fitted) / root_weight) * norm_scale
    working = jnp.concatenate([scaled, target[None, :]], axis=0)
    blocks = []
    for step in range(NPAN):
        panel_rows = working[:PB]
        trailing = working[PB:]
        lower_factor = jnp.linalg.cholesky(inner_rows(panel_rows, panel_rows))
        orthonormal = lax.linalg.triangular_solve(lower_factor, panel_rows, left_side=True, lower=True)
        coupling = inner_rows(orthonormal, trailing)
        working = trailing - jnp.dot(coupling.T, orthonormal, precision=precise)
        blocks.append(jnp.concatenate([jnp.zeros((PB, step * PB), jnp.float32), lower_factor.T, coupling[:, :-1]], axis=1))
    return (jnp.concatenate(blocks, axis=0), working[0] * math.sqrt(ROWS))
```

```python
import math

import jax
import jax.numpy as jnp
from jax import lax
from jax.sharding import PartitionSpec as P

PB = 64


precise = lax.Precision.HIGHEST


def shards(features, labels, other_predictor, coefficients, panel_block):
    window, rows_here = features.shape
    total_rows = rows_here * lax.axis_size("row")
    first_col = panel_block[0] * PB
    window_coef = lax.dynamic_slice(coefficients, (first_col,), (window,))
    as_float = features.astype(jnp.float32)
    linear = jnp.dot(window_coef, as_float, precision=precise) + other_predictor
    fitted = jax.nn.sigmoid(linear)
    weight = jnp.maximum(fitted * (1.0 - fitted), 0.01)
    root_weight = jnp.sqrt(weight)
    norm_scale = 1.0 / math.sqrt(total_rows)
    scaled = as_float * (root_weight * norm_scale)[None, :]
    target = (
        root_weight * linear + (labels.astype(jnp.float32) - fitted) / root_weight
    ) * norm_scale
    working = jnp.concatenate([scaled, target[None, :]], axis=0)
    local_gram = lax.dot_general(
        working, working, (((1,), (1,)), ((), ())), precision=precise
    )
    gram = lax.psum(local_gram, "row")
    lower = jnp.linalg.cholesky(gram)
    lower_window = lower[:window, :window]
    projection = lower[window, :window]
    coef = lax.linalg.triangular_solve(
        lower_window, projection[:, None], left_side=True, lower=True, transpose_a=True
    )[:, 0]
    fitted_part = jnp.dot(coef, scaled, precision=precise)
    residual = (target - fitted_part) * math.sqrt(total_rows)
    return lower_window.T, residual


def solution(mesh):
    in_specs = (
        P(None, ("groups", "row")),
        P(("groups", "row")),
        P(("groups", "row")),
        P("groups"),
        P("groups"),
    )
    out_specs = (P("groups", None), P(("groups", "row")))
    return jax.shard_map(shards, mesh=mesh, in_specs=in_specs, out_specs=out_specs, check_vma=False)
```

```python
import math

import jax
import jax.numpy as jnp
from jax import lax
from jax.sharding import PartitionSpec as P

PB = 64


precise = lax.Precision.HIGHEST


def butterfly_sum(flat, axis):
    size = lax.axis_size(axis)
    steps = size.bit_length() - 1
    me = lax.axis_index(axis)
    current = flat
    for bit in range(steps):
        half = current.shape[0] // 2
        low, high = current[:half], current[half:]
        upper_half = ((me >> bit) & 1) == 1
        send = jnp.where(upper_half, low, high)
        keep = jnp.where(upper_half, high, low)
        pairs = [(i, i ^ (1 << bit)) for i in range(size)]
        current = keep + lax.ppermute(send, axis, pairs)
    for bit in reversed(range(steps)):
        pairs = [(i, i ^ (1 << bit)) for i in range(size)]
        got = lax.ppermute(current, axis, pairs)
        upper_half = ((me >> bit) & 1) == 1
        current = jnp.where(
            upper_half, jnp.concatenate([got, current]), jnp.concatenate([current, got])
        )
    return current


def shards(features, labels, other_predictor, coefficients, panel_block):
    window, rows_here = features.shape
    row_devices = lax.axis_size("row")
    assert row_devices & (row_devices - 1) == 0
    total_rows = rows_here * row_devices
    first_col = panel_block[0] * PB
    window_coef = lax.dynamic_slice(coefficients, (first_col,), (window,))
    as_float = features.astype(jnp.float32)
    linear = jnp.dot(window_coef, as_float, precision=precise) + other_predictor
    fitted = jax.nn.sigmoid(linear)
    weight = jnp.maximum(fitted * (1.0 - fitted), 0.01)
    root_weight = jnp.sqrt(weight)
    norm_scale = 1.0 / math.sqrt(total_rows)
    scaled = as_float * (root_weight * norm_scale)[None, :]
    target = (
        root_weight * linear + (labels.astype(jnp.float32) - fitted) / root_weight
    ) * norm_scale
    working = jnp.concatenate([scaled, target[None, :]], axis=0)
    width = window + 1
    local_gram = lax.dot_general(
        working, working, (((1,), (1,)), ((), ())), precision=precise
    )
    panels = window // PB
    pieces = [local_gram[k * PB:(k + 1) * PB, :(k + 1) * PB].reshape(-1) for k in range(panels)]
    pieces.append(local_gram[window])
    used = sum(p.shape[0] for p in pieces)
    quantum = row_devices * 128
    padded = -(-used // quantum) * quantum
    pieces.append(jnp.zeros((padded - used,), jnp.float32))
    packed = butterfly_sum(jnp.concatenate(pieces), "row")
    lower_gram = jnp.zeros((width, width), jnp.float32)
    offset = 0
    for k in range(panels):
        block = packed[offset:offset + PB * (k + 1) * PB].reshape(PB, (k + 1) * PB)
        lower_gram = lower_gram.at[k * PB:(k + 1) * PB, :(k + 1) * PB].set(block)
        offset += PB * (k + 1) * PB
    lower_gram = lower_gram.at[window].set(packed[offset:offset + width])
    lower = lax.linalg.cholesky(lower_gram, symmetrize_input=False)
    lower_window = lower[:window, :window]
    projection = lower[window, :window]
    coef = lax.linalg.triangular_solve(
        lower_window, projection[:, None], left_side=True, lower=True, transpose_a=True
    )[:, 0]
    fitted_part = jnp.dot(coef, scaled, precision=precise)
    residual = (target - fitted_part) * math.sqrt(total_rows)
    return lower_window.T, residual


def solution(mesh):
    in_specs = (
        P(None, ("groups", "row")),
        P(("groups", "row")),
        P(("groups", "row")),
        P("groups"),
        P("groups"),
    )
    out_specs = (P("groups", None), P(("groups", "row")))
    return jax.shard_map(shards, mesh=mesh, in_specs=in_specs, out_specs=out_specs, check_vma=False)
```

```python
import functools
import math

import jax
import jax.numpy as jnp
from jax import lax
from jax.experimental import pallas as pl
from jax.experimental.pallas import tpu as pltpu
from jax.sharding import PartitionSpec as P

PB = 64


precise = lax.Precision.HIGHEST


BLOCK = 128


def nt(a, b):
    return lax.dot_general(a, b, (((1,), (1,)), ((), ())), precision=precise, preferred_element_type=jnp.float32)


def nn(a, b):
    return lax.dot_general(a, b, (((1,), (0,)), ((), ())), precision=precise, preferred_element_type=jnp.float32)


def chol_kernel(g_ref, l_ref, z_ref, d_ref, m_ref, k_ref, *, blocks, last_steps, target):
    b = BLOCK
    lane = lax.broadcasted_iota(jnp.int32, (b, b), 1)
    sub = lax.broadcasted_iota(jnp.int32, (b, b), 0)
    lane_row = lax.broadcasted_iota(jnp.int32, (1, b), 1)
    sub_col = lax.broadcasted_iota(jnp.int32, (b, 1), 0)
    eye = jnp.where(lane == sub, 1.0, 0.0).astype(jnp.float32)
    l_ref[...] = g_ref[...]
    inverses = []
    for k in range(blocks):
        r0 = k * b
        d_ref[...] = l_ref[r0:r0 + b, r0:r0 + b]
        m_ref[...] = eye
        k_ref[...] = jnp.zeros((b, b), jnp.float32)

        def step(j, carry):
            d = d_ref[...]
            col = jnp.sum(jnp.where(lane == j, d, 0.0), axis=1, keepdims=True)
            piv = jnp.sum(jnp.where(sub_col == j, col, 0.0), axis=0, keepdims=True)
            inv = lax.rsqrt(piv)
            lcol = jnp.where(sub_col >= j, col * inv, 0.0)
            lrow = jnp.where(lane_row >= j, d_ref[pl.ds(j, 1), :] * inv, 0.0)
            d_ref[...] = d - lcol * lrow
            k_ref[...] = jnp.where(lane == j, lcol, k_ref[...])
            mrow = m_ref[pl.ds(j, 1), :] * inv
            below = jnp.where(sub_col > j, lcol, 0.0)
            m_ref[...] = jnp.where(sub == j, mrow, m_ref[...] - below * mrow)
            return carry

        steps = b if k < blocks - 1 else last_steps
        lax.fori_loop(0, steps, step, 0)
        inverse = m_ref[...]
        inverses.append(inverse)
        l_ref[r0:r0 + b, r0:r0 + b] = k_ref[...]
        if k < blocks - 1:
            panel = nt(l_ref[r0 + b:, r0:r0 + b], inverse)
            l_ref[r0 + b:, r0:r0 + b] = panel
            l_ref[r0 + b:, r0 + b:] = l_ref[r0 + b:, r0 + b:] - nt(panel, panel)
            l_ref[r0:r0 + b, r0 + b:] = jnp.zeros((b, l_ref.shape[1] - r0 - b), jnp.float32)
    last = blocks - 1
    tl = target - last * b
    lane8 = lax.broadcasted_iota(jnp.int32, (8, b), 1)
    row = l_ref[pl.ds(target, 1), :]
    zs = [None] * blocks
    for k in range(last, -1, -1):
        acc = jnp.broadcast_to(row[:, k * b:(k + 1) * b], (8, b))
        if k == last:
            acc = jnp.where(lane8 < tl, acc, 0.0)
        for i in range(k + 1, blocks):
            acc = acc - nn(zs[i], l_ref[i * b:(i + 1) * b, k * b:(k + 1) * b])
        zk = nn(acc, inverses[k])
        if k == last:
            zk = jnp.where(lane8 < tl, zk, 0.0)
        zs[k] = zk
        z_ref[:, k * b:(k + 1) * b] = zk


def cholesky_and_solve(sym, target):
    n = sym.shape[0]
    blocks = n // BLOCK
    last_steps = target + 1 - (blocks - 1) * BLOCK
    kernel = functools.partial(chol_kernel, blocks=blocks, last_steps=last_steps, target=target)
    vmem = pltpu.VMEM
    return pl.pallas_call(
        kernel,
        out_shape=(jax.ShapeDtypeStruct((n, n), jnp.float32), jax.ShapeDtypeStruct((8, n), jnp.float32)),
        in_specs=[pl.BlockSpec(memory_space=vmem)],
        out_specs=(pl.BlockSpec(memory_space=vmem), pl.BlockSpec(memory_space=vmem)),
        scratch_shapes=[pltpu.VMEM((BLOCK, BLOCK), jnp.float32)] * 3,
    )(sym)


def butterfly_sum(flat, axis):
    size = lax.axis_size(axis)
    steps = size.bit_length() - 1
    me = lax.axis_index(axis)
    current = flat
    for bit in range(steps):
        half = current.shape[0] // 2
        low, high = current[:half], current[half:]
        upper_half = ((me >> bit) & 1) == 1
        send = jnp.where(upper_half, low, high)
        keep = jnp.where(upper_half, high, low)
        pairs = [(i, i ^ (1 << bit)) for i in range(size)]
        current = keep + lax.ppermute(send, axis, pairs)
    for bit in reversed(range(steps)):
        pairs = [(i, i ^ (1 << bit)) for i in range(size)]
        got = lax.ppermute(current, axis, pairs)
        upper_half = ((me >> bit) & 1) == 1
        current = jnp.where(
            upper_half, jnp.concatenate([got, current]), jnp.concatenate([current, got])
        )
    return current


def shards(features, labels, other_predictor, coefficients, panel_block):
    window, rows_here = features.shape
    row_devices = lax.axis_size("row")
    assert row_devices & (row_devices - 1) == 0
    total_rows = rows_here * row_devices
    first_col = panel_block[0] * PB
    window_coef = lax.dynamic_slice(coefficients, (first_col,), (window,))
    as_float = features.astype(jnp.float32)
    linear = jnp.dot(window_coef, as_float, precision=precise) + other_predictor
    fitted = jax.nn.sigmoid(linear)
    weight = jnp.maximum(fitted * (1.0 - fitted), 0.01)
    root_weight = jnp.sqrt(weight)
    norm_scale = 1.0 / math.sqrt(total_rows)
    scaled = as_float * (root_weight * norm_scale)[None, :]
    target = (
        root_weight * linear + (labels.astype(jnp.float32) - fitted) / root_weight
    ) * norm_scale
    working = jnp.concatenate([scaled, target[None, :]], axis=0)
    width = window + 1
    local_gram = lax.dot_general(
        working, working, (((1,), (1,)), ((), ())), precision=precise
    )
    panels = window // PB
    pieces = [local_gram[k * PB:(k + 1) * PB, :(k + 1) * PB].reshape(-1) for k in range(panels)]
    pieces.append(local_gram[window])
    used = sum(p.shape[0] for p in pieces)
    quantum = row_devices * 128
    padded = -(-used // quantum) * quantum
    pieces.append(jnp.zeros((padded - used,), jnp.float32))
    packed = butterfly_sum(jnp.concatenate(pieces), "row")
    size = -(-width // BLOCK) * BLOCK
    lower_gram = jnp.zeros((size, size), jnp.float32)
    offset = 0
    for k in range(panels):
        block = packed[offset:offset + PB * (k + 1) * PB].reshape(PB, (k + 1) * PB)
        lower_gram = lower_gram.at[k * PB:(k + 1) * PB, :(k + 1) * PB].set(block)
        offset += PB * (k + 1) * PB
    lower_gram = lower_gram.at[window, :width].set(packed[offset:offset + width])
    rows = lax.broadcasted_iota(jnp.int32, (size, size), 0)
    cols = lax.broadcasted_iota(jnp.int32, (size, size), 1)
    sym = jnp.where(rows >= cols, lower_gram, lower_gram.T)
    sym = jnp.where((rows == cols) & (rows >= width), 1.0, sym)
    lower, solved = cholesky_and_solve(sym, window)
    lower_window = lower[:window, :window]
    coef = solved[0, :window]
    fitted_part = jnp.dot(coef, scaled, precision=precise)
    residual = (target - fitted_part) * math.sqrt(total_rows)
    return lower_window.T, residual


def solution(mesh):
    in_specs = (
        P(None, ("groups", "row")),
        P(("groups", "row")),
        P(("groups", "row")),
        P("groups"),
        P("groups"),
    )
    out_specs = (P("groups", None), P(("groups", "row")))
    return jax.shard_map(shards, mesh=mesh, in_specs=in_specs, out_specs=out_specs, check_vma=False)
```

```python
import functools
import math

import jax
import jax.numpy as jnp
from jax import lax
from jax.experimental import pallas as pl
from jax.experimental.pallas import tpu as pltpu
from jax.sharding import PartitionSpec as P

PB = 64


precise = lax.Precision.HIGHEST


BLOCK = 128


def nt(a, b):
    return lax.dot_general(a, b, (((1,), (1,)), ((), ())), precision=precise, preferred_element_type=jnp.float32)


def nn(a, b):
    return lax.dot_general(a, b, (((1,), (0,)), ((), ())), precision=precise, preferred_element_type=jnp.float32)


def chol_kernel(g_ref, l_ref, z_ref, d_ref, m_ref, k_ref, *, blocks, last_steps, target):
    b = BLOCK
    lane = lax.broadcasted_iota(jnp.int32, (b, b), 1)
    sub = lax.broadcasted_iota(jnp.int32, (b, b), 0)
    lane_row = lax.broadcasted_iota(jnp.int32, (1, b), 1)
    sub_col = lax.broadcasted_iota(jnp.int32, (b, 1), 0)
    eye = jnp.where(lane == sub, 1.0, 0.0).astype(jnp.float32)
    index = 0
    for i in range(blocks):
        for k in range(blocks):
            if k <= i:
                l_ref[i * b:(i + 1) * b, k * b:(k + 1) * b] = g_ref[index * b:(index + 1) * b, :]
                index += 1
            else:
                l_ref[i * b:(i + 1) * b, k * b:(k + 1) * b] = jnp.zeros((b, b), jnp.float32)
    inverses = []
    for k in range(blocks):
        r0 = k * b
        d_ref[...] = l_ref[r0:r0 + b, r0:r0 + b]
        m_ref[...] = eye
        k_ref[...] = jnp.zeros((b, b), jnp.float32)

        def step(j, carry):
            d = d_ref[...]
            col = jnp.sum(jnp.where(lane == j, d, 0.0), axis=1, keepdims=True)
            piv = jnp.sum(jnp.where(sub_col == j, col, 0.0), axis=0, keepdims=True)
            inv = lax.rsqrt(piv)
            lcol = jnp.where(sub_col >= j, col * inv, 0.0)
            lrow = jnp.where(lane_row >= j, d_ref[pl.ds(j, 1), :] * inv, 0.0)
            d_ref[...] = d - lcol * lrow
            k_ref[...] = jnp.where(lane == j, lcol, k_ref[...])
            mrow = m_ref[pl.ds(j, 1), :] * inv
            below = jnp.where(sub_col > j, lcol, 0.0)
            m_ref[...] = jnp.where(sub == j, mrow, m_ref[...] - below * mrow)
            return carry

        steps = b if k < blocks - 1 else last_steps
        lax.fori_loop(0, steps, step, 0)
        inverse = m_ref[...]
        inverses.append(inverse)
        l_ref[r0:r0 + b, r0:r0 + b] = k_ref[...]
        if k < blocks - 1:
            panel = nt(l_ref[r0 + b:, r0:r0 + b], inverse)
            l_ref[r0 + b:, r0:r0 + b] = panel
            l_ref[r0 + b:, r0 + b:] = l_ref[r0 + b:, r0 + b:] - nt(panel, panel)
            l_ref[r0:r0 + b, r0 + b:] = jnp.zeros((b, l_ref.shape[1] - r0 - b), jnp.float32)
    last = blocks - 1
    tl = target - last * b
    lane8 = lax.broadcasted_iota(jnp.int32, (8, b), 1)
    row = l_ref[pl.ds(target, 1), :]
    zs = [None] * blocks
    for k in range(last, -1, -1):
        acc = jnp.broadcast_to(row[:, k * b:(k + 1) * b], (8, b))
        if k == last:
            acc = jnp.where(lane8 < tl, acc, 0.0)
        for i in range(k + 1, blocks):
            acc = acc - nn(zs[i], l_ref[i * b:(i + 1) * b, k * b:(k + 1) * b])
        zk = nn(acc, inverses[k])
        if k == last:
            zk = jnp.where(lane8 < tl, zk, 0.0)
        zs[k] = zk
        z_ref[:, k * b:(k + 1) * b] = zk


def cholesky_and_solve(sym, target, blocks):
    n = blocks * BLOCK
    last_steps = target + 1 - (blocks - 1) * BLOCK
    kernel = functools.partial(chol_kernel, blocks=blocks, last_steps=last_steps, target=target)
    vmem = pltpu.VMEM
    return pl.pallas_call(
        kernel,
        out_shape=(jax.ShapeDtypeStruct((n, n), jnp.float32), jax.ShapeDtypeStruct((8, n), jnp.float32)),
        in_specs=[pl.BlockSpec(memory_space=vmem)],
        out_specs=(pl.BlockSpec(memory_space=vmem), pl.BlockSpec(memory_space=vmem)),
        scratch_shapes=[pltpu.VMEM((BLOCK, BLOCK), jnp.float32)] * 3,
    )(sym)


def butterfly_sum(flat, axis):
    size = lax.axis_size(axis)
    steps = size.bit_length() - 1
    me = lax.axis_index(axis)
    current = flat
    for bit in range(steps):
        half = current.shape[0] // 2
        low, high = current[:half], current[half:]
        upper_half = ((me >> bit) & 1) == 1
        send = jnp.where(upper_half, low, high)
        keep = jnp.where(upper_half, high, low)
        pairs = [(i, i ^ (1 << bit)) for i in range(size)]
        current = keep + lax.ppermute(send, axis, pairs)
    for bit in reversed(range(steps)):
        pairs = [(i, i ^ (1 << bit)) for i in range(size)]
        got = lax.ppermute(current, axis, pairs)
        upper_half = ((me >> bit) & 1) == 1
        current = jnp.where(
            upper_half, jnp.concatenate([got, current]), jnp.concatenate([current, got])
        )
    return current


def shards(features, labels, other_predictor, coefficients, panel_block):
    window, rows_here = features.shape
    row_devices = lax.axis_size("row")
    assert row_devices & (row_devices - 1) == 0
    total_rows = rows_here * row_devices
    first_col = panel_block[0] * PB
    window_coef = lax.dynamic_slice(coefficients, (first_col,), (window,))
    as_float = features.astype(jnp.float32)
    linear = jnp.dot(window_coef, as_float, precision=precise) + other_predictor
    fitted = jax.nn.sigmoid(linear)
    weight = jnp.maximum(fitted * (1.0 - fitted), 0.01)
    root_weight = jnp.sqrt(weight)
    norm_scale = 1.0 / math.sqrt(total_rows)
    scaled = as_float * (root_weight * norm_scale)[None, :]
    target = (
        root_weight * linear + (labels.astype(jnp.float32) - fitted) / root_weight
    ) * norm_scale
    working = jnp.concatenate([scaled, target[None, :]], axis=0)
    width = window + 1
    blocks = -(-width // BLOCK)
    size = blocks * BLOCK
    working = jnp.concatenate([working, jnp.zeros((size - width, rows_here), jnp.float32)], axis=0)
    local_gram = lax.dot_general(
        working, working, (((1,), (1,)), ((), ())), precision=precise
    )
    pieces = [
        local_gram[i * BLOCK:(i + 1) * BLOCK, k * BLOCK:(k + 1) * BLOCK]
        for i in range(blocks)
        for k in range(i + 1)
    ]
    used = len(pieces) * BLOCK
    quantum = row_devices * 8
    padded = -(-used // quantum) * quantum
    if padded > used:
        pieces.append(jnp.zeros((padded - used, BLOCK), jnp.float32))
    packed = butterfly_sum(jnp.concatenate(pieces, axis=0), "row")
    lower, solved = cholesky_and_solve(packed, window, blocks)
    lower_window = lower[:window, :window]
    coef = solved[0, :window]
    fitted_part = jnp.dot(coef, scaled, precision=precise)
    residual = (target - fitted_part) * math.sqrt(total_rows)
    return lower_window.T, residual


def solution(mesh):
    in_specs = (
        P(None, ("groups", "row")),
        P(("groups", "row")),
        P(("groups", "row")),
        P("groups"),
        P("groups"),
    )
    out_specs = (P("groups", None), P(("groups", "row")))
    return jax.shard_map(shards, mesh=mesh, in_specs=in_specs, out_specs=out_specs, check_vma=False)
```

```python
import functools
import math

import jax
import jax.numpy as jnp
from jax import lax
from jax.experimental import pallas as pl
from jax.experimental.pallas import tpu as pltpu
from jax.sharding import PartitionSpec as P

PB = 64


precise = lax.Precision.HIGHEST


BLOCK = 128


def nt(a, b):
    return lax.dot_general(a, b, (((1,), (1,)), ((), ())), precision=precise, preferred_element_type=jnp.float32)


def nn(a, b):
    return lax.dot_general(a, b, (((1,), (0,)), ((), ())), precision=precise, preferred_element_type=jnp.float32)


def chol_kernel(g_ref, l_ref, z_ref, d_ref, m_ref, k_ref, *, blocks, last_steps, target):
    b = BLOCK
    lane = lax.broadcasted_iota(jnp.int32, (b, b), 1)
    sub = lax.broadcasted_iota(jnp.int32, (b, b), 0)
    lane_row = lax.broadcasted_iota(jnp.int32, (1, b), 1)
    sub_col = lax.broadcasted_iota(jnp.int32, (b, 1), 0)
    eye = jnp.where(lane == sub, 1.0, 0.0).astype(jnp.float32)
    index = 0
    for i in range(blocks):
        for k in range(blocks):
            if k <= i:
                l_ref[i * b:(i + 1) * b, k * b:(k + 1) * b] = g_ref[index * b:(index + 1) * b, :]
                index += 1
            else:
                l_ref[i * b:(i + 1) * b, k * b:(k + 1) * b] = jnp.zeros((b, b), jnp.float32)
    inverses = []
    for k in range(blocks):
        r0 = k * b
        d_ref[...] = l_ref[r0:r0 + b, r0:r0 + b]
        m_ref[...] = eye
        k_ref[...] = jnp.zeros((b, b), jnp.float32)

        steps = b if k < blocks - 1 else last_steps
        for tile in range(-(-steps // 8)):
            top = tile * 8
            rows = b - top
            lane_t = lane[top:, :]
            sub_t = sub[top:, :]
            sub_col_t = sub_col[top:, :]

            def step(j, carry, top=top, lane_t=lane_t, sub_t=sub_t, sub_col_t=sub_col_t):
                d = d_ref[top:, :]
                col = jnp.sum(jnp.where(lane_t == j, d, 0.0), axis=1, keepdims=True)
                piv = jnp.sum(jnp.where(sub_col_t == j, col, 0.0), axis=0, keepdims=True)
                inv = lax.rsqrt(piv)
                lcol = jnp.where(sub_col_t >= j, col * inv, 0.0)
                lrow = jnp.where(lane_row >= j, d_ref[pl.ds(j, 1), :] * inv, 0.0)
                d_ref[top:, :] = d - lcol * lrow
                k_ref[pl.ds(j, 1), :] = lrow
                mrow = m_ref[pl.ds(j, 1), :] * inv
                below = jnp.where(sub_col_t > j, lcol, 0.0)
                m_ref[top:, :] = jnp.where(sub_t == j, mrow, m_ref[top:, :] - below * mrow)
                return carry

            lax.fori_loop(top, min(top + 8, steps), step, 0)
        inverse = m_ref[...]
        inverses.append(inverse)
        l_ref[r0:r0 + b, r0:r0 + b] = k_ref[...].T
        if k < blocks - 1:
            panel = nt(l_ref[r0 + b:, r0:r0 + b], inverse)
            l_ref[r0 + b:, r0:r0 + b] = panel
            l_ref[r0 + b:, r0 + b:] = l_ref[r0 + b:, r0 + b:] - nt(panel, panel)
            l_ref[r0:r0 + b, r0 + b:] = jnp.zeros((b, l_ref.shape[1] - r0 - b), jnp.float32)
    last = blocks - 1
    tl = target - last * b
    lane8 = lax.broadcasted_iota(jnp.int32, (8, b), 1)
    row = l_ref[pl.ds(target, 1), :]
    zs = [None] * blocks
    for k in range(last, -1, -1):
        acc = jnp.broadcast_to(row[:, k * b:(k + 1) * b], (8, b))
        if k == last:
            acc = jnp.where(lane8 < tl, acc, 0.0)
        for i in range(k + 1, blocks):
            acc = acc - nn(zs[i], l_ref[i * b:(i + 1) * b, k * b:(k + 1) * b])
        zk = nn(acc, inverses[k])
        if k == last:
            zk = jnp.where(lane8 < tl, zk, 0.0)
        zs[k] = zk
        z_ref[:, k * b:(k + 1) * b] = zk


def cholesky_and_solve(sym, target, blocks):
    n = blocks * BLOCK
    last_steps = target + 1 - (blocks - 1) * BLOCK
    kernel = functools.partial(chol_kernel, blocks=blocks, last_steps=last_steps, target=target)
    vmem = pltpu.VMEM
    return pl.pallas_call(
        kernel,
        out_shape=(jax.ShapeDtypeStruct((n, n), jnp.float32), jax.ShapeDtypeStruct((8, n), jnp.float32)),
        in_specs=[pl.BlockSpec(memory_space=vmem)],
        out_specs=(pl.BlockSpec(memory_space=vmem), pl.BlockSpec(memory_space=vmem)),
        scratch_shapes=[pltpu.VMEM((BLOCK, BLOCK), jnp.float32)] * 3,
    )(sym)


def butterfly_sum(flat, axis):
    size = lax.axis_size(axis)
    steps = size.bit_length() - 1
    me = lax.axis_index(axis)
    current = flat
    for bit in range(steps):
        half = current.shape[0] // 2
        low, high = current[:half], current[half:]
        upper_half = ((me >> bit) & 1) == 1
        send = jnp.where(upper_half, low, high)
        keep = jnp.where(upper_half, high, low)
        pairs = [(i, i ^ (1 << bit)) for i in range(size)]
        current = keep + lax.ppermute(send, axis, pairs)
    for bit in reversed(range(steps)):
        pairs = [(i, i ^ (1 << bit)) for i in range(size)]
        got = lax.ppermute(current, axis, pairs)
        upper_half = ((me >> bit) & 1) == 1
        current = jnp.where(
            upper_half, jnp.concatenate([got, current]), jnp.concatenate([current, got])
        )
    return current


def shards(features, labels, other_predictor, coefficients, panel_block):
    window, rows_here = features.shape
    row_devices = lax.axis_size("row")
    assert row_devices & (row_devices - 1) == 0
    total_rows = rows_here * row_devices
    first_col = panel_block[0] * PB
    window_coef = lax.dynamic_slice(coefficients, (first_col,), (window,))
    as_float = features.astype(jnp.float32)
    linear = jnp.dot(window_coef, as_float, precision=precise) + other_predictor
    fitted = jax.nn.sigmoid(linear)
    weight = jnp.maximum(fitted * (1.0 - fitted), 0.01)
    root_weight = jnp.sqrt(weight)
    norm_scale = 1.0 / math.sqrt(total_rows)
    scaled = as_float * (root_weight * norm_scale)[None, :]
    target = (
        root_weight * linear + (labels.astype(jnp.float32) - fitted) / root_weight
    ) * norm_scale
    working = jnp.concatenate([scaled, target[None, :]], axis=0)
    width = window + 1
    blocks = -(-width // BLOCK)
    size = blocks * BLOCK
    working = jnp.concatenate([working, jnp.zeros((size - width, rows_here), jnp.float32)], axis=0)
    local_gram = lax.dot_general(
        working, working, (((1,), (1,)), ((), ())), precision=precise
    )
    pieces = [
        local_gram[i * BLOCK:(i + 1) * BLOCK, k * BLOCK:(k + 1) * BLOCK]
        for i in range(blocks)
        for k in range(i + 1)
    ]
    used = len(pieces) * BLOCK
    quantum = row_devices * 8
    padded = -(-used // quantum) * quantum
    if padded > used:
        pieces.append(jnp.zeros((padded - used, BLOCK), jnp.float32))
    packed = butterfly_sum(jnp.concatenate(pieces, axis=0), "row")
    lower, solved = cholesky_and_solve(packed, window, blocks)
    lower_window = lower[:window, :window]
    coef = solved[0, :window]
    fitted_part = jnp.dot(coef, scaled, precision=precise)
    residual = (target - fitted_part) * math.sqrt(total_rows)
    return lower_window.T, residual


def solution(mesh):
    in_specs = (
        P(None, ("groups", "row")),
        P(("groups", "row")),
        P(("groups", "row")),
        P("groups"),
        P("groups"),
    )
    out_specs = (P("groups", None), P(("groups", "row")))
    return jax.shard_map(shards, mesh=mesh, in_specs=in_specs, out_specs=out_specs, check_vma=False)
```

```python
import functools
import math

import jax
import jax.numpy as jnp
from jax import lax
from jax.experimental import pallas as pl
from jax.experimental.pallas import tpu as pltpu
from jax.sharding import PartitionSpec as P

PB = 64


precise = lax.Precision.HIGHEST


BLOCK = 128


def nt(a, b):
    return lax.dot_general(a, b, (((1,), (1,)), ((), ())), precision=precise, preferred_element_type=jnp.float32)


def nn(a, b):
    return lax.dot_general(a, b, (((1,), (0,)), ((), ())), precision=precise, preferred_element_type=jnp.float32)


def chol_kernel(g_ref, l_ref, z_ref, d_ref, m_ref, k_ref, *, blocks, last_steps, target):
    b = BLOCK
    lane = lax.broadcasted_iota(jnp.int32, (b, b), 1)
    sub = lax.broadcasted_iota(jnp.int32, (b, b), 0)
    lane_row = lax.broadcasted_iota(jnp.int32, (1, b), 1)
    sub_col = lax.broadcasted_iota(jnp.int32, (b, 1), 0)
    eye = jnp.where(lane == sub, 1.0, 0.0).astype(jnp.float32)
    index = 0
    for i in range(blocks):
        for k in range(blocks):
            if k <= i:
                l_ref[i * b:(i + 1) * b, k * b:(k + 1) * b] = g_ref[index * b:(index + 1) * b, :]
                index += 1
            else:
                l_ref[i * b:(i + 1) * b, k * b:(k + 1) * b] = jnp.zeros((b, b), jnp.float32)
    inverses = []
    for k in range(blocks):
        r0 = k * b
        d_ref[...] = l_ref[r0:r0 + b, r0:r0 + b]
        m_ref[...] = eye
        k_ref[...] = jnp.zeros((b, b), jnp.float32)

        steps = b if k < blocks - 1 else last_steps
        column = jnp.sum(jnp.where(lane == 0, d_ref[...], 0.0), axis=1, keepdims=True)
        for tile in range(-(-steps // 8)):
            top = tile * 8
            lane_t = lane[top:, :]
            sub_t = sub[top:, :]
            sub_col_t = sub_col[top:, :]

            def step(j, c, top=top, lane_t=lane_t, sub_t=sub_t, sub_col_t=sub_col_t):
                d = d_ref[top:, :]
                ahead = jnp.sum(jnp.where(lane_t == j + 1, d, 0.0), axis=1, keepdims=True)
                piv = jnp.sum(jnp.where(sub_col_t == j, c, 0.0), axis=0, keepdims=True)
                nxt = jnp.sum(jnp.where(sub_col_t == j + 1, c, 0.0), axis=0, keepdims=True)
                inv = lax.rsqrt(piv)
                live = jnp.where(sub_col_t >= j, c, 0.0)
                lcol = live * inv
                lrow = jnp.where(lane_row >= j, d_ref[pl.ds(j, 1), :] * inv, 0.0)
                d_ref[top:, :] = d - lcol * lrow
                k_ref[pl.ds(j, 1), :] = lrow
                mrow = m_ref[pl.ds(j, 1), :] * inv
                below = jnp.where(sub_col_t > j, lcol, 0.0)
                m_ref[top:, :] = jnp.where(sub_t == j, mrow, m_ref[top:, :] - below * mrow)
                return ahead - live * (nxt / piv)

            column = lax.fori_loop(top, min(top + 8, steps), step, column)
            column = column[8:]
        inverse = m_ref[...]
        inverses.append(inverse)
        l_ref[r0:r0 + b, r0:r0 + b] = k_ref[...].T
        if k < blocks - 1:
            panel = nt(l_ref[r0 + b:, r0:r0 + b], inverse)
            l_ref[r0 + b:, r0:r0 + b] = panel
            l_ref[r0 + b:, r0 + b:] = l_ref[r0 + b:, r0 + b:] - nt(panel, panel)
            l_ref[r0:r0 + b, r0 + b:] = jnp.zeros((b, l_ref.shape[1] - r0 - b), jnp.float32)
    last = blocks - 1
    tl = target - last * b
    lane8 = lax.broadcasted_iota(jnp.int32, (8, b), 1)
    row = l_ref[pl.ds(target, 1), :]
    zs = [None] * blocks
    for k in range(last, -1, -1):
        acc = jnp.broadcast_to(row[:, k * b:(k + 1) * b], (8, b))
        if k == last:
            acc = jnp.where(lane8 < tl, acc, 0.0)
        for i in range(k + 1, blocks):
            acc = acc - nn(zs[i], l_ref[i * b:(i + 1) * b, k * b:(k + 1) * b])
        zk = nn(acc, inverses[k])
        if k == last:
            zk = jnp.where(lane8 < tl, zk, 0.0)
        zs[k] = zk
        z_ref[:, k * b:(k + 1) * b] = zk


def cholesky_and_solve(sym, target, blocks):
    n = blocks * BLOCK
    last_steps = target + 1 - (blocks - 1) * BLOCK
    kernel = functools.partial(chol_kernel, blocks=blocks, last_steps=last_steps, target=target)
    vmem = pltpu.VMEM
    return pl.pallas_call(
        kernel,
        out_shape=(jax.ShapeDtypeStruct((n, n), jnp.float32), jax.ShapeDtypeStruct((8, n), jnp.float32)),
        in_specs=[pl.BlockSpec(memory_space=vmem)],
        out_specs=(pl.BlockSpec(memory_space=vmem), pl.BlockSpec(memory_space=vmem)),
        scratch_shapes=[pltpu.VMEM((BLOCK, BLOCK), jnp.float32)] * 3,
    )(sym)


def butterfly_sum(flat, axis):
    size = lax.axis_size(axis)
    steps = size.bit_length() - 1
    me = lax.axis_index(axis)
    current = flat
    for bit in range(steps):
        half = current.shape[0] // 2
        low, high = current[:half], current[half:]
        upper_half = ((me >> bit) & 1) == 1
        send = jnp.where(upper_half, low, high)
        keep = jnp.where(upper_half, high, low)
        pairs = [(i, i ^ (1 << bit)) for i in range(size)]
        current = keep + lax.ppermute(send, axis, pairs)
    for bit in reversed(range(steps)):
        pairs = [(i, i ^ (1 << bit)) for i in range(size)]
        got = lax.ppermute(current, axis, pairs)
        upper_half = ((me >> bit) & 1) == 1
        current = jnp.where(
            upper_half, jnp.concatenate([got, current]), jnp.concatenate([current, got])
        )
    return current


def shards(features, labels, other_predictor, coefficients, panel_block):
    window, rows_here = features.shape
    row_devices = lax.axis_size("row")
    assert row_devices & (row_devices - 1) == 0
    total_rows = rows_here * row_devices
    first_col = panel_block[0] * PB
    window_coef = lax.dynamic_slice(coefficients, (first_col,), (window,))
    as_float = features.astype(jnp.float32)
    linear = jnp.dot(window_coef, as_float, precision=precise) + other_predictor
    fitted = jax.nn.sigmoid(linear)
    weight = jnp.maximum(fitted * (1.0 - fitted), 0.01)
    root_weight = jnp.sqrt(weight)
    norm_scale = 1.0 / math.sqrt(total_rows)
    scaled = as_float * (root_weight * norm_scale)[None, :]
    target = (
        root_weight * linear + (labels.astype(jnp.float32) - fitted) / root_weight
    ) * norm_scale
    working = jnp.concatenate([scaled, target[None, :]], axis=0)
    width = window + 1
    blocks = -(-width // BLOCK)
    size = blocks * BLOCK
    working = jnp.concatenate([working, jnp.zeros((size - width, rows_here), jnp.float32)], axis=0)
    local_gram = lax.dot_general(
        working, working, (((1,), (1,)), ((), ())), precision=precise
    )
    pieces = [
        local_gram[i * BLOCK:(i + 1) * BLOCK, k * BLOCK:(k + 1) * BLOCK]
        for i in range(blocks)
        for k in range(i + 1)
    ]
    used = len(pieces) * BLOCK
    quantum = row_devices * 8
    padded = -(-used // quantum) * quantum
    if padded > used:
        pieces.append(jnp.zeros((padded - used, BLOCK), jnp.float32))
    packed = butterfly_sum(jnp.concatenate(pieces, axis=0), "row")
    lower, solved = cholesky_and_solve(packed, window, blocks)
    lower_window = lower[:window, :window]
    coef = solved[0, :window]
    fitted_part = jnp.dot(coef, scaled, precision=precise)
    residual = (target - fitted_part) * math.sqrt(total_rows)
    return lower_window.T, residual


def solution(mesh):
    in_specs = (
        P(None, ("groups", "row")),
        P(("groups", "row")),
        P(("groups", "row")),
        P("groups"),
        P("groups"),
    )
    out_specs = (P("groups", None), P(("groups", "row")))
    return jax.shard_map(shards, mesh=mesh, in_specs=in_specs, out_specs=out_specs, check_vma=False)
```

```python
import functools
import math

import jax
import jax.numpy as jnp
from jax import lax
from jax.experimental import pallas as pl
from jax.experimental.pallas import tpu as pltpu
from jax.sharding import PartitionSpec as P

PB = 64


precise = lax.Precision.HIGHEST


BLOCK = 128


def nt(a, b):
    return lax.dot_general(a, b, (((1,), (1,)), ((), ())), precision=precise, preferred_element_type=jnp.float32)


def nn(a, b):
    return lax.dot_general(a, b, (((1,), (0,)), ((), ())), precision=precise, preferred_element_type=jnp.float32)


def chol_kernel(g_ref, l_ref, z_ref, d_ref, m_ref, k_ref, *, blocks, last_steps, target):
    b = BLOCK
    lane = lax.broadcasted_iota(jnp.int32, (b, b), 1)
    sub = lax.broadcasted_iota(jnp.int32, (b, b), 0)
    lane_row = lax.broadcasted_iota(jnp.int32, (1, b), 1)
    sub_col = lax.broadcasted_iota(jnp.int32, (b, 1), 0)
    eye = jnp.where(lane == sub, 1.0, 0.0).astype(jnp.float32)
    index = 0
    for i in range(blocks):
        for k in range(blocks):
            if k <= i:
                l_ref[i * b:(i + 1) * b, k * b:(k + 1) * b] = g_ref[index * b:(index + 1) * b, :]
                index += 1
            else:
                l_ref[i * b:(i + 1) * b, k * b:(k + 1) * b] = jnp.zeros((b, b), jnp.float32)
    inverses = []
    for k in range(blocks):
        r0 = k * b
        d_ref[...] = l_ref[r0:r0 + b, r0:r0 + b]
        m_ref[...] = eye
        k_ref[...] = jnp.zeros((b, b), jnp.float32)

        steps = b if k < blocks - 1 else last_steps
        column = jnp.sum(jnp.where(lane == 0, d_ref[...], 0.0), axis=1, keepdims=True)
        for tile in range(-(-steps // 8)):
            top = tile * 8
            lane_t = lane[top:, :]
            sub_t = sub[top:, :]
            sub_col_t = sub_col[top:, :]

            def step(j, c, top=top, lane_t=lane_t, sub_t=sub_t, sub_col_t=sub_col_t):
                d = d_ref[top:, :]
                ahead = jnp.sum(jnp.where(lane_t == j + 1, d, 0.0), axis=1, keepdims=True)
                lead = min(16, b - top)
                piv = jnp.sum(jnp.where(sub_col_t[:lead] == j, c[:lead], 0.0), axis=0, keepdims=True)
                nxt = jnp.sum(jnp.where(sub_col_t[:lead] == j + 1, c[:lead], 0.0), axis=0, keepdims=True)
                inv = lax.rsqrt(piv)
                live = jnp.where(sub_col_t >= j, c, 0.0)
                lcol = live * inv
                lrow = jnp.where(lane_row >= j, d_ref[pl.ds(j, 1), :] * inv, 0.0)
                d_ref[top:, :] = d - lcol * lrow
                k_ref[pl.ds(j, 1), :] = lrow
                mrow = m_ref[pl.ds(j, 1), :] * inv
                below = jnp.where(sub_col_t > j, lcol, 0.0)
                m_ref[top:, :] = jnp.where(sub_t == j, mrow, m_ref[top:, :] - below * mrow)
                return ahead - live * (nxt / piv)

            column = lax.fori_loop(top, min(top + 8, steps), step, column)
            column = column[8:]
        inverse = m_ref[...]
        inverses.append(inverse)
        l_ref[r0:r0 + b, r0:r0 + b] = k_ref[...].T
        if k < blocks - 1:
            panel = nt(l_ref[r0 + b:, r0:r0 + b], inverse)
            l_ref[r0 + b:, r0:r0 + b] = panel
            l_ref[r0 + b:, r0 + b:] = l_ref[r0 + b:, r0 + b:] - nt(panel, panel)
            l_ref[r0:r0 + b, r0 + b:] = jnp.zeros((b, l_ref.shape[1] - r0 - b), jnp.float32)
    last = blocks - 1
    tl = target - last * b
    lane8 = lax.broadcasted_iota(jnp.int32, (8, b), 1)
    row = l_ref[pl.ds(target, 1), :]
    zs = [None] * blocks
    for k in range(last, -1, -1):
        acc = jnp.broadcast_to(row[:, k * b:(k + 1) * b], (8, b))
        if k == last:
            acc = jnp.where(lane8 < tl, acc, 0.0)
        for i in range(k + 1, blocks):
            acc = acc - nn(zs[i], l_ref[i * b:(i + 1) * b, k * b:(k + 1) * b])
        zk = nn(acc, inverses[k])
        if k == last:
            zk = jnp.where(lane8 < tl, zk, 0.0)
        zs[k] = zk
        z_ref[:, k * b:(k + 1) * b] = zk


def cholesky_and_solve(sym, target, blocks):
    n = blocks * BLOCK
    last_steps = target + 1 - (blocks - 1) * BLOCK
    kernel = functools.partial(chol_kernel, blocks=blocks, last_steps=last_steps, target=target)
    vmem = pltpu.VMEM
    return pl.pallas_call(
        kernel,
        out_shape=(jax.ShapeDtypeStruct((n, n), jnp.float32), jax.ShapeDtypeStruct((8, n), jnp.float32)),
        in_specs=[pl.BlockSpec(memory_space=vmem)],
        out_specs=(pl.BlockSpec(memory_space=vmem), pl.BlockSpec(memory_space=vmem)),
        scratch_shapes=[pltpu.VMEM((BLOCK, BLOCK), jnp.float32)] * 3,
    )(sym)


def butterfly_sum(flat, axis):
    size = lax.axis_size(axis)
    steps = size.bit_length() - 1
    me = lax.axis_index(axis)
    current = flat
    for bit in range(steps):
        half = current.shape[0] // 2
        low, high = current[:half], current[half:]
        upper_half = ((me >> bit) & 1) == 1
        send = jnp.where(upper_half, low, high)
        keep = jnp.where(upper_half, high, low)
        pairs = [(i, i ^ (1 << bit)) for i in range(size)]
        current = keep + lax.ppermute(send, axis, pairs)
    for bit in reversed(range(steps)):
        pairs = [(i, i ^ (1 << bit)) for i in range(size)]
        got = lax.ppermute(current, axis, pairs)
        upper_half = ((me >> bit) & 1) == 1
        current = jnp.where(
            upper_half, jnp.concatenate([got, current]), jnp.concatenate([current, got])
        )
    return current


def shards(features, labels, other_predictor, coefficients, panel_block):
    window, rows_here = features.shape
    row_devices = lax.axis_size("row")
    assert row_devices & (row_devices - 1) == 0
    total_rows = rows_here * row_devices
    first_col = panel_block[0] * PB
    window_coef = lax.dynamic_slice(coefficients, (first_col,), (window,))
    as_float = features.astype(jnp.float32)
    linear = jnp.dot(window_coef, as_float, precision=precise) + other_predictor
    fitted = jax.nn.sigmoid(linear)
    weight = jnp.maximum(fitted * (1.0 - fitted), 0.01)
    root_weight = jnp.sqrt(weight)
    norm_scale = 1.0 / math.sqrt(total_rows)
    scaled = as_float * (root_weight * norm_scale)[None, :]
    target = (
        root_weight * linear + (labels.astype(jnp.float32) - fitted) / root_weight
    ) * norm_scale
    working = jnp.concatenate([scaled, target[None, :]], axis=0)
    width = window + 1
    blocks = -(-width // BLOCK)
    size = blocks * BLOCK
    working = jnp.concatenate([working, jnp.zeros((size - width, rows_here), jnp.float32)], axis=0)
    local_gram = lax.dot_general(
        working, working, (((1,), (1,)), ((), ())), precision=precise
    )
    pieces = [
        local_gram[i * BLOCK:(i + 1) * BLOCK, k * BLOCK:(k + 1) * BLOCK]
        for i in range(blocks)
        for k in range(i + 1)
    ]
    used = len(pieces) * BLOCK
    quantum = row_devices * 8
    padded = -(-used // quantum) * quantum
    if padded > used:
        pieces.append(jnp.zeros((padded - used, BLOCK), jnp.float32))
    packed = butterfly_sum(jnp.concatenate(pieces, axis=0), "row")
    lower, solved = cholesky_and_solve(packed, window, blocks)
    lower_window = lower[:window, :window]
    coef = solved[0, :window]
    fitted_part = jnp.dot(coef, scaled, precision=precise)
    residual = (target - fitted_part) * math.sqrt(total_rows)
    return lower_window.T, residual


def solution(mesh):
    in_specs = (
        P(None, ("groups", "row")),
        P(("groups", "row")),
        P(("groups", "row")),
        P("groups"),
        P("groups"),
    )
    out_specs = (P("groups", None), P(("groups", "row")))
    return jax.shard_map(shards, mesh=mesh, in_specs=in_specs, out_specs=out_specs, check_vma=False)
```

```python
import functools
import math

import jax
import jax.numpy as jnp
from jax import lax
from jax.experimental import pallas as pl
from jax.experimental.pallas import tpu as pltpu
from jax.sharding import PartitionSpec as P

PB = 64


precise = lax.Precision.HIGHEST


BLOCK = 128


def nt(a, b):
    return lax.dot_general(a, b, (((1,), (1,)), ((), ())), precision=precise, preferred_element_type=jnp.float32)


def nn(a, b):
    return lax.dot_general(a, b, (((1,), (0,)), ((), ())), precision=precise, preferred_element_type=jnp.float32)


def chol_kernel(g_ref, l_ref, z_ref, d_ref, m_ref, k_ref, *, blocks, last_steps, target):
    b = BLOCK
    lane = lax.broadcasted_iota(jnp.int32, (b, b), 1)
    sub = lax.broadcasted_iota(jnp.int32, (b, b), 0)
    lane_row = lax.broadcasted_iota(jnp.int32, (1, b), 1)
    sub_col = lax.broadcasted_iota(jnp.int32, (b, 1), 0)
    eye = jnp.where(lane == sub, 1.0, 0.0).astype(jnp.float32)
    index = 0
    for i in range(blocks):
        for k in range(blocks):
            if k <= i:
                l_ref[i * b:(i + 1) * b, k * b:(k + 1) * b] = g_ref[index * b:(index + 1) * b, :]
                index += 1
            else:
                l_ref[i * b:(i + 1) * b, k * b:(k + 1) * b] = jnp.zeros((b, b), jnp.float32)
    inverses = []
    for k in range(blocks):
        r0 = k * b
        d_ref[...] = l_ref[r0:r0 + b, r0:r0 + b]
        m_ref[...] = eye
        k_ref[...] = jnp.zeros((b, b), jnp.float32)

        steps = b if k < blocks - 1 else last_steps
        column = jnp.sum(jnp.where(lane == 0, d_ref[...], 0.0), axis=1, keepdims=True)
        for tile in range(-(-steps // 8)):
            top = tile * 8
            lane_t = lane[top:, :]
            sub_t = sub[top:, :]
            sub_col_t = sub_col[top:, :]

            def step(j, c, top=top, lane_t=lane_t, sub_t=sub_t, sub_col_t=sub_col_t):
                d = d_ref[top:, :]
                ahead = jnp.sum(jnp.where(lane_t == j + 1, d, 0.0), axis=1, keepdims=True)
                lead = min(16, b - top)
                piv = jnp.sum(jnp.where(sub_col_t[:lead] == j, c[:lead], 0.0), axis=0, keepdims=True)
                nxt = jnp.sum(jnp.where(sub_col_t[:lead] == j + 1, c[:lead], 0.0), axis=0, keepdims=True)
                inv = lax.rsqrt(piv)
                live = jnp.where(sub_col_t >= j, c, 0.0)
                lcol = live * inv
                lrow = jnp.where(lane_row >= j, d_ref[pl.ds(j, 1), :] * inv, 0.0)
                d_ref[top:, :] = d - lcol * lrow
                k_ref[pl.ds(j, 1), :] = lrow
                mrow = m_ref[pl.ds(j, 1), :] * inv
                below = jnp.where(sub_col_t > j, lcol, 0.0)
                m_ref[top:, :] = jnp.where(sub_t == j, mrow, m_ref[top:, :] - below * mrow)
                return ahead - live * (nxt / piv)

            column = lax.fori_loop(top, min(top + 8, steps), step, column, unroll=True)
            column = column[8:]
        inverse = m_ref[...]
        inverses.append(inverse)
        l_ref[r0:r0 + b, r0:r0 + b] = k_ref[...].T
        if k < blocks - 1:
            panel = nt(l_ref[r0 + b:, r0:r0 + b], inverse)
            l_ref[r0 + b:, r0:r0 + b] = panel
            l_ref[r0 + b:, r0 + b:] = l_ref[r0 + b:, r0 + b:] - nt(panel, panel)
            l_ref[r0:r0 + b, r0 + b:] = jnp.zeros((b, l_ref.shape[1] - r0 - b), jnp.float32)
    last = blocks - 1
    tl = target - last * b
    lane8 = lax.broadcasted_iota(jnp.int32, (8, b), 1)
    row = l_ref[pl.ds(target, 1), :]
    zs = [None] * blocks
    for k in range(last, -1, -1):
        acc = jnp.broadcast_to(row[:, k * b:(k + 1) * b], (8, b))
        if k == last:
            acc = jnp.where(lane8 < tl, acc, 0.0)
        for i in range(k + 1, blocks):
            acc = acc - nn(zs[i], l_ref[i * b:(i + 1) * b, k * b:(k + 1) * b])
        zk = nn(acc, inverses[k])
        if k == last:
            zk = jnp.where(lane8 < tl, zk, 0.0)
        zs[k] = zk
        z_ref[:, k * b:(k + 1) * b] = zk


def cholesky_and_solve(sym, target, blocks):
    n = blocks * BLOCK
    last_steps = target + 1 - (blocks - 1) * BLOCK
    kernel = functools.partial(chol_kernel, blocks=blocks, last_steps=last_steps, target=target)
    vmem = pltpu.VMEM
    return pl.pallas_call(
        kernel,
        out_shape=(jax.ShapeDtypeStruct((n, n), jnp.float32), jax.ShapeDtypeStruct((8, n), jnp.float32)),
        in_specs=[pl.BlockSpec(memory_space=vmem)],
        out_specs=(pl.BlockSpec(memory_space=vmem), pl.BlockSpec(memory_space=vmem)),
        scratch_shapes=[pltpu.VMEM((BLOCK, BLOCK), jnp.float32)] * 3,
    )(sym)


def butterfly_sum(flat, axis):
    size = lax.axis_size(axis)
    steps = size.bit_length() - 1
    me = lax.axis_index(axis)
    current = flat
    for bit in range(steps):
        half = current.shape[0] // 2
        low, high = current[:half], current[half:]
        upper_half = ((me >> bit) & 1) == 1
        send = jnp.where(upper_half, low, high)
        keep = jnp.where(upper_half, high, low)
        pairs = [(i, i ^ (1 << bit)) for i in range(size)]
        current = keep + lax.ppermute(send, axis, pairs)
    for bit in reversed(range(steps)):
        pairs = [(i, i ^ (1 << bit)) for i in range(size)]
        got = lax.ppermute(current, axis, pairs)
        upper_half = ((me >> bit) & 1) == 1
        current = jnp.where(
            upper_half, jnp.concatenate([got, current]), jnp.concatenate([current, got])
        )
    return current


def shards(features, labels, other_predictor, coefficients, panel_block):
    window, rows_here = features.shape
    row_devices = lax.axis_size("row")
    assert row_devices & (row_devices - 1) == 0
    total_rows = rows_here * row_devices
    first_col = panel_block[0] * PB
    window_coef = lax.dynamic_slice(coefficients, (first_col,), (window,))
    as_float = features.astype(jnp.float32)
    linear = jnp.dot(window_coef, as_float, precision=precise) + other_predictor
    fitted = jax.nn.sigmoid(linear)
    weight = jnp.maximum(fitted * (1.0 - fitted), 0.01)
    root_weight = jnp.sqrt(weight)
    norm_scale = 1.0 / math.sqrt(total_rows)
    scaled = as_float * (root_weight * norm_scale)[None, :]
    target = (
        root_weight * linear + (labels.astype(jnp.float32) - fitted) / root_weight
    ) * norm_scale
    working = jnp.concatenate([scaled, target[None, :]], axis=0)
    width = window + 1
    blocks = -(-width // BLOCK)
    size = blocks * BLOCK
    working = jnp.concatenate([working, jnp.zeros((size - width, rows_here), jnp.float32)], axis=0)
    local_gram = lax.dot_general(
        working, working, (((1,), (1,)), ((), ())), precision=precise
    )
    pieces = [
        local_gram[i * BLOCK:(i + 1) * BLOCK, k * BLOCK:(k + 1) * BLOCK]
        for i in range(blocks)
        for k in range(i + 1)
    ]
    used = len(pieces) * BLOCK
    quantum = row_devices * 8
    padded = -(-used // quantum) * quantum
    if padded > used:
        pieces.append(jnp.zeros((padded - used, BLOCK), jnp.float32))
    packed = butterfly_sum(jnp.concatenate(pieces, axis=0), "row")
    lower, solved = cholesky_and_solve(packed, window, blocks)
    lower_window = lower[:window, :window]
    coef = solved[0, :window]
    fitted_part = jnp.dot(coef, scaled, precision=precise)
    residual = (target - fitted_part) * math.sqrt(total_rows)
    return lower_window.T, residual


def solution(mesh):
    in_specs = (
        P(None, ("groups", "row")),
        P(("groups", "row")),
        P(("groups", "row")),
        P("groups"),
        P("groups"),
    )
    out_specs = (P("groups", None), P(("groups", "row")))
    return jax.shard_map(shards, mesh=mesh, in_specs=in_specs, out_specs=out_specs, check_vma=False)
```

```python
import functools
import math

import jax
import jax.numpy as jnp
from jax import lax
from jax.experimental import pallas as pl
from jax.experimental.pallas import tpu as pltpu
from jax.sharding import PartitionSpec as P

PB = 64


precise = lax.Precision.HIGHEST


BLOCK = 128


def nt(a, b):
    return lax.dot_general(a, b, (((1,), (1,)), ((), ())), precision=precise, preferred_element_type=jnp.float32)


def nn(a, b):
    return lax.dot_general(a, b, (((1,), (0,)), ((), ())), precision=precise, preferred_element_type=jnp.float32)


def chol_kernel(g_ref, l_ref, z_ref, d_ref, m_ref, k_ref, *, blocks, last_steps, target):
    b = BLOCK
    lane = lax.broadcasted_iota(jnp.int32, (b, b), 1)
    sub = lax.broadcasted_iota(jnp.int32, (b, b), 0)
    lane_row = lax.broadcasted_iota(jnp.int32, (1, b), 1)
    sub_col = lax.broadcasted_iota(jnp.int32, (b, 1), 0)
    eye = jnp.where(lane == sub, 1.0, 0.0).astype(jnp.float32)
    index = 0
    for i in range(blocks):
        for k in range(blocks):
            if k <= i:
                l_ref[i * b:(i + 1) * b, k * b:(k + 1) * b] = g_ref[index * b:(index + 1) * b, :]
                index += 1
            else:
                l_ref[i * b:(i + 1) * b, k * b:(k + 1) * b] = jnp.zeros((b, b), jnp.float32)
    inverses = []
    for k in range(blocks):
        r0 = k * b
        d_ref[...] = l_ref[r0:r0 + b, r0:r0 + b]
        m_ref[...] = eye
        k_ref[...] = jnp.zeros((b, b), jnp.float32)

        steps = b if k < blocks - 1 else last_steps
        column = jnp.sum(jnp.where(lane == 0, d_ref[...], 0.0), axis=1, keepdims=True)
        for tile in range(-(-steps // 8)):
            top = tile * 8
            lane_t = lane[top:, :]
            sub_t = sub[top:, :]
            sub_col_t = sub_col[top:, :]

            def step(j, c, top=top, lane_t=lane_t, sub_t=sub_t, sub_col_t=sub_col_t):
                d = d_ref[top:, :]
                ahead = jnp.sum(jnp.where(lane_t == j + 1, d, 0.0), axis=1, keepdims=True)
                lead = min(16, b - top)
                piv = jnp.sum(jnp.where(sub_col_t[:lead] == j, c[:lead], 0.0), axis=0, keepdims=True)
                nxt = jnp.sum(jnp.where(sub_col_t[:lead] == j + 1, c[:lead], 0.0), axis=0, keepdims=True)
                inv = lax.rsqrt(piv)
                live = jnp.where(sub_col_t >= j, c, 0.0)
                lcol = live * inv
                lrow = jnp.where(lane_row >= j, d_ref[pl.ds(j, 1), :] * inv, 0.0)
                d_ref[top:, :] = d - lcol * lrow
                k_ref[pl.ds(j, 1), :] = lrow
                mrow = m_ref[pl.ds(j, 1), :] * inv
                below = jnp.where(sub_col_t > j, lcol, 0.0)
                m_ref[top:, :] = jnp.where(sub_t == j, mrow, m_ref[top:, :] - below * mrow)
                return ahead - live * (nxt / piv)

            column = lax.fori_loop(top, min(top + 8, steps), step, column, unroll=True)
            column = column[8:]
        inverse = m_ref[...]
        inverses.append(inverse)
        l_ref[r0:r0 + b, r0:r0 + b] = k_ref[...].T
        if k < blocks - 1:
            panel = nt(l_ref[r0 + b:, r0:r0 + b], inverse)
            l_ref[r0 + b:, r0:r0 + b] = panel
            l_ref[r0 + b:, r0 + b:] = l_ref[r0 + b:, r0 + b:] - nt(panel, panel)
            l_ref[r0:r0 + b, r0 + b:] = jnp.zeros((b, l_ref.shape[1] - r0 - b), jnp.float32)
    last = blocks - 1
    tl = target - last * b
    lane8 = lax.broadcasted_iota(jnp.int32, (8, b), 1)
    row = l_ref[pl.ds(target, 1), :]
    zs = [None] * blocks
    for k in range(last, -1, -1):
        acc = jnp.broadcast_to(row[:, k * b:(k + 1) * b], (8, b))
        if k == last:
            acc = jnp.where(lane8 < tl, acc, 0.0)
        for i in range(k + 1, blocks):
            acc = acc - nn(zs[i], l_ref[i * b:(i + 1) * b, k * b:(k + 1) * b])
        zk = nn(acc, inverses[k])
        if k == last:
            zk = jnp.where(lane8 < tl, zk, 0.0)
        zs[k] = zk
        z_ref[:, k * b:(k + 1) * b] = zk


def cholesky_and_solve(sym, target, blocks):
    n = blocks * BLOCK
    last_steps = target + 1 - (blocks - 1) * BLOCK
    kernel = functools.partial(chol_kernel, blocks=blocks, last_steps=last_steps, target=target)
    vmem = pltpu.VMEM
    return pl.pallas_call(
        kernel,
        out_shape=(jax.ShapeDtypeStruct((n, n), jnp.float32), jax.ShapeDtypeStruct((8, n), jnp.float32)),
        in_specs=[pl.BlockSpec(memory_space=vmem)],
        out_specs=(pl.BlockSpec(memory_space=vmem), pl.BlockSpec(memory_space=vmem)),
        scratch_shapes=[pltpu.VMEM((BLOCK, BLOCK), jnp.float32)] * 3,
    )(sym)


def butterfly_sum(flat, axis, order):
    size = lax.axis_size(axis)
    steps = size.bit_length() - 1
    me = lax.axis_index(axis)
    current = flat
    for bit in order:
        half = current.shape[0] // 2
        low, high = current[:half], current[half:]
        upper_half = ((me >> bit) & 1) == 1
        send = jnp.where(upper_half, low, high)
        keep = jnp.where(upper_half, high, low)
        pairs = [(i, i ^ (1 << bit)) for i in range(size)]
        current = keep + lax.ppermute(send, axis, pairs)
    for bit in reversed(order):
        pairs = [(i, i ^ (1 << bit)) for i in range(size)]
        got = lax.ppermute(current, axis, pairs)
        upper_half = ((me >> bit) & 1) == 1
        current = jnp.where(
            upper_half, jnp.concatenate([got, current]), jnp.concatenate([current, got])
        )
    return current


def shards(features, labels, other_predictor, coefficients, panel_block):
    window, rows_here = features.shape
    row_devices = lax.axis_size("row")
    assert row_devices & (row_devices - 1) == 0
    total_rows = rows_here * row_devices
    first_col = panel_block[0] * PB
    window_coef = lax.dynamic_slice(coefficients, (first_col,), (window,))
    as_float = features.astype(jnp.float32)
    linear = jnp.dot(window_coef, as_float, precision=precise) + other_predictor
    fitted = jax.nn.sigmoid(linear)
    weight = jnp.maximum(fitted * (1.0 - fitted), 0.01)
    root_weight = jnp.sqrt(weight)
    norm_scale = 1.0 / math.sqrt(total_rows)
    scaled = as_float * (root_weight * norm_scale)[None, :]
    target = (
        root_weight * linear + (labels.astype(jnp.float32) - fitted) / root_weight
    ) * norm_scale
    working = jnp.concatenate([scaled, target[None, :]], axis=0)
    width = window + 1
    blocks = -(-width // BLOCK)
    size = blocks * BLOCK
    working = jnp.concatenate([working, jnp.zeros((size - width, rows_here), jnp.float32)], axis=0)
    local_gram = lax.dot_general(
        working, working, (((1,), (1,)), ((), ())), precision=precise
    )
    pieces = [
        local_gram[i * BLOCK:(i + 1) * BLOCK, k * BLOCK:(k + 1) * BLOCK]
        for i in range(blocks)
        for k in range(i + 1)
    ]
    used = len(pieces) * BLOCK
    quantum = row_devices * 8
    padded = -(-used // quantum) * quantum
    if padded > used:
        pieces.append(jnp.zeros((padded - used, BLOCK), jnp.float32))
    stacked = jnp.concatenate(pieces, axis=0)
    steps = row_devices.bit_length() - 1
    first = list(range(steps))
    second = [0, 2, 1] + first[3:] if steps >= 3 else first
    half = padded // 2
    packed = jnp.concatenate(
        [butterfly_sum(stacked[:half], "row", first), butterfly_sum(stacked[half:], "row", second)], axis=0
    )
    lower, solved = cholesky_and_solve(packed, window, blocks)
    lower_window = lower[:window, :window]
    coef = solved[0, :window]
    fitted_part = jnp.dot(coef, scaled, precision=precise)
    residual = (target - fitted_part) * math.sqrt(total_rows)
    return lower_window.T, residual


def solution(mesh):
    in_specs = (
        P(None, ("groups", "row")),
        P(("groups", "row")),
        P(("groups", "row")),
        P("groups"),
        P("groups"),
    )
    out_specs = (P("groups", None), P(("groups", "row")))
    return jax.shard_map(shards, mesh=mesh, in_specs=in_specs, out_specs=out_specs, check_vma=False)
```

```python
import functools
import math

import jax
import jax.numpy as jnp
from jax import lax
from jax.experimental import pallas as pl
from jax.experimental.pallas import tpu as pltpu
from jax.sharding import PartitionSpec as P

PB = 64


precise = lax.Precision.HIGHEST


BLOCK = 128


def nt(a, b):
    return lax.dot_general(a, b, (((1,), (1,)), ((), ())), precision=precise, preferred_element_type=jnp.float32)


def nn(a, b):
    return lax.dot_general(a, b, (((1,), (0,)), ((), ())), precision=precise, preferred_element_type=jnp.float32)


def chol_kernel(g_ref, l_ref, z_ref, d_ref, m_ref, k_ref, *, blocks, last_steps, target):
    b = BLOCK
    lane = lax.broadcasted_iota(jnp.int32, (b, b), 1)
    sub = lax.broadcasted_iota(jnp.int32, (b, b), 0)
    lane_row = lax.broadcasted_iota(jnp.int32, (1, b), 1)
    sub_col = lax.broadcasted_iota(jnp.int32, (b, 1), 0)
    eye = jnp.where(lane == sub, 1.0, 0.0).astype(jnp.float32)
    index = 0
    for i in range(blocks):
        for k in range(blocks):
            if k <= i:
                l_ref[i * b:(i + 1) * b, k * b:(k + 1) * b] = g_ref[index * b:(index + 1) * b, :]
                index += 1
            else:
                l_ref[i * b:(i + 1) * b, k * b:(k + 1) * b] = jnp.zeros((b, b), jnp.float32)
    inverses = []
    for k in range(blocks):
        r0 = k * b
        d_ref[...] = l_ref[r0:r0 + b, r0:r0 + b]
        m_ref[...] = eye
        k_ref[...] = jnp.zeros((b, b), jnp.float32)

        steps = b if k < blocks - 1 else last_steps
        column = jnp.broadcast_to(d_ref[:, 0:1], (b, b))
        for tile in range(-(-steps // 8)):
            top = tile * 8
            sub_t = sub[top:, :]
            for j in range(top, min(top + 8, steps)):
                r = j - top
                d = d_ref[top:, :]
                piv = column[r:r + 1, :]
                inv = lax.rsqrt(piv)
                live = jnp.where(sub_t >= j, column, 0.0)
                lcol = live * inv
                lrow = jnp.where(lane_row >= j, d[r:r + 1, :] * inv, 0.0)
                d_ref[top:, :] = d - lcol * lrow
                k_ref[j:j + 1, :] = lrow
                mrow = m_ref[j:j + 1, :] * inv
                below = jnp.where(sub_t > j, lcol, 0.0)
                m_ref[top:, :] = jnp.where(sub_t == j, mrow, m_ref[top:, :] - below * mrow)
                if j + 1 < steps:
                    ahead = jnp.broadcast_to(d[:, j + 1:j + 2], d.shape)
                    column = ahead - live * (column[r + 1:r + 2, :] / piv)
            column = column[8:]
        inverse = m_ref[...]
        inverses.append(inverse)
        l_ref[r0:r0 + b, r0:r0 + b] = k_ref[...].T
        if k < blocks - 1:
            panel = nt(l_ref[r0 + b:, r0:r0 + b], inverse)
            l_ref[r0 + b:, r0:r0 + b] = panel
            l_ref[r0 + b:, r0 + b:] = l_ref[r0 + b:, r0 + b:] - nt(panel, panel)
            l_ref[r0:r0 + b, r0 + b:] = jnp.zeros((b, l_ref.shape[1] - r0 - b), jnp.float32)
    last = blocks - 1
    tl = target - last * b
    lane8 = lax.broadcasted_iota(jnp.int32, (8, b), 1)
    row = l_ref[pl.ds(target, 1), :]
    zs = [None] * blocks
    for k in range(last, -1, -1):
        acc = jnp.broadcast_to(row[:, k * b:(k + 1) * b], (8, b))
        if k == last:
            acc = jnp.where(lane8 < tl, acc, 0.0)
        for i in range(k + 1, blocks):
            acc = acc - nn(zs[i], l_ref[i * b:(i + 1) * b, k * b:(k + 1) * b])
        zk = nn(acc, inverses[k])
        if k == last:
            zk = jnp.where(lane8 < tl, zk, 0.0)
        zs[k] = zk
        z_ref[:, k * b:(k + 1) * b] = zk


def cholesky_and_solve(sym, target, blocks):
    n = blocks * BLOCK
    last_steps = target + 1 - (blocks - 1) * BLOCK
    kernel = functools.partial(chol_kernel, blocks=blocks, last_steps=last_steps, target=target)
    vmem = pltpu.VMEM
    return pl.pallas_call(
        kernel,
        out_shape=(jax.ShapeDtypeStruct((n, n), jnp.float32), jax.ShapeDtypeStruct((8, n), jnp.float32)),
        in_specs=[pl.BlockSpec(memory_space=vmem)],
        out_specs=(pl.BlockSpec(memory_space=vmem), pl.BlockSpec(memory_space=vmem)),
        scratch_shapes=[pltpu.VMEM((BLOCK, BLOCK), jnp.float32)] * 3,
    )(sym)


def butterfly_sum(flat, axis, order):
    size = lax.axis_size(axis)
    steps = size.bit_length() - 1
    me = lax.axis_index(axis)
    current = flat
    for bit in order:
        half = current.shape[0] // 2
        low, high = current[:half], current[half:]
        upper_half = ((me >> bit) & 1) == 1
        send = jnp.where(upper_half, low, high)
        keep = jnp.where(upper_half, high, low)
        pairs = [(i, i ^ (1 << bit)) for i in range(size)]
        current = keep + lax.ppermute(send, axis, pairs)
    for bit in reversed(order):
        pairs = [(i, i ^ (1 << bit)) for i in range(size)]
        got = lax.ppermute(current, axis, pairs)
        upper_half = ((me >> bit) & 1) == 1
        current = jnp.where(
            upper_half, jnp.concatenate([got, current]), jnp.concatenate([current, got])
        )
    return current


def shards(features, labels, other_predictor, coefficients, panel_block):
    window, rows_here = features.shape
    row_devices = lax.axis_size("row")
    assert row_devices & (row_devices - 1) == 0
    total_rows = rows_here * row_devices
    first_col = panel_block[0] * PB
    window_coef = lax.dynamic_slice(coefficients, (first_col,), (window,))
    as_float = features.astype(jnp.float32)
    linear = jnp.dot(window_coef, as_float, precision=precise) + other_predictor
    fitted = jax.nn.sigmoid(linear)
    weight = jnp.maximum(fitted * (1.0 - fitted), 0.01)
    root_weight = jnp.sqrt(weight)
    norm_scale = 1.0 / math.sqrt(total_rows)
    scaled = as_float * (root_weight * norm_scale)[None, :]
    target = (
        root_weight * linear + (labels.astype(jnp.float32) - fitted) / root_weight
    ) * norm_scale
    working = jnp.concatenate([scaled, target[None, :]], axis=0)
    width = window + 1
    blocks = -(-width // BLOCK)
    size = blocks * BLOCK
    working = jnp.concatenate([working, jnp.zeros((size - width, rows_here), jnp.float32)], axis=0)
    local_gram = lax.dot_general(
        working, working, (((1,), (1,)), ((), ())), precision=precise
    )
    pieces = [
        local_gram[i * BLOCK:(i + 1) * BLOCK, k * BLOCK:(k + 1) * BLOCK]
        for i in range(blocks)
        for k in range(i + 1)
    ]
    used = len(pieces) * BLOCK
    quantum = row_devices * 8
    padded = -(-used // quantum) * quantum
    if padded > used:
        pieces.append(jnp.zeros((padded - used, BLOCK), jnp.float32))
    stacked = jnp.concatenate(pieces, axis=0)
    steps = row_devices.bit_length() - 1
    first = list(range(steps))
    second = [0, 2, 1] + first[3:] if steps >= 3 else first
    half = padded // 2
    packed = jnp.concatenate(
        [butterfly_sum(stacked[:half], "row", first), butterfly_sum(stacked[half:], "row", second)], axis=0
    )
    lower, solved = cholesky_and_solve(packed, window, blocks)
    lower_window = lower[:window, :window]
    coef = solved[0, :window]
    fitted_part = jnp.dot(coef, scaled, precision=precise)
    residual = (target - fitted_part) * math.sqrt(total_rows)
    return lower_window.T, residual


def solution(mesh):
    in_specs = (
        P(None, ("groups", "row")),
        P(("groups", "row")),
        P(("groups", "row")),
        P("groups"),
        P("groups"),
    )
    out_specs = (P("groups", None), P(("groups", "row")))
    return jax.shard_map(shards, mesh=mesh, in_specs=in_specs, out_specs=out_specs, check_vma=False)
```

```python
import functools
import math

import jax
import jax.numpy as jnp
from jax import lax
from jax.experimental import pallas as pl
from jax.experimental.pallas import tpu as pltpu
from jax.sharding import PartitionSpec as P

PB = 64


precise = lax.Precision.HIGHEST


BLOCK = 128


def nt(a, b):
    return lax.dot_general(a, b, (((1,), (1,)), ((), ())), precision=precise, preferred_element_type=jnp.float32)


def nn(a, b):
    return lax.dot_general(a, b, (((1,), (0,)), ((), ())), precision=precise, preferred_element_type=jnp.float32)


def chol_kernel(g_ref, l_ref, z_ref, d_ref, m_ref, k_ref, *, blocks, last_steps, target):
    b = BLOCK
    lane = lax.broadcasted_iota(jnp.int32, (b, b), 1)
    sub = lax.broadcasted_iota(jnp.int32, (b, b), 0)
    lane_row = lax.broadcasted_iota(jnp.int32, (1, b), 1)
    sub_col = lax.broadcasted_iota(jnp.int32, (b, 1), 0)
    eye = jnp.where(lane == sub, 1.0, 0.0).astype(jnp.float32)
    index = 0
    for i in range(blocks):
        for k in range(blocks):
            if k <= i:
                l_ref[i * b:(i + 1) * b, k * b:(k + 1) * b] = g_ref[index * b:(index + 1) * b, :]
                index += 1
            else:
                l_ref[i * b:(i + 1) * b, k * b:(k + 1) * b] = jnp.zeros((b, b), jnp.float32)
    inverses = []
    for k in range(blocks):
        r0 = k * b
        d_ref[...] = l_ref[r0:r0 + b, r0:r0 + b]
        m_ref[...] = eye
        k_ref[...] = jnp.zeros((b, b), jnp.float32)

        steps = b if k < blocks - 1 else last_steps
        column = jnp.broadcast_to(d_ref[:, 0:1], (b, b))
        for tile in range(-(-steps // 8)):
            top = tile * 8
            sub_t = sub[top:, :]
            for j in range(top, min(top + 8, steps)):
                r = j - top
                d = d_ref[top:, :]
                piv = column[r:r + 1, :]
                inv = lax.rsqrt(piv)
                live = jnp.where(sub_t >= j, column, 0.0)
                lcol = live * inv
                lrow = jnp.where(lane_row >= j, d[r:r + 1, :] * inv, 0.0)
                d_ref[top:, :] = d - lcol * lrow
                k_ref[j:j + 1, :] = lrow
                mrow = m_ref[j:j + 1, :] * inv
                below = jnp.where(sub_t > j, lcol, 0.0)
                m_ref[top:, :] = jnp.where(sub_t == j, mrow, m_ref[top:, :] - below * mrow)
                if j + 1 < steps:
                    ahead = jnp.broadcast_to(d[:, j + 1:j + 2], d.shape)
                    column = ahead - live * (column[r + 1:r + 2, :] / piv)
            column = column[8:]
        inverse = m_ref[...]
        inverses.append(inverse)
        l_ref[r0:r0 + b, r0:r0 + b] = k_ref[...].T
        if k < blocks - 1:
            panel = nt(l_ref[r0 + b:, r0:r0 + b], inverse)
            l_ref[r0 + b:, r0:r0 + b] = panel
            for i in range(k + 1, blocks):
                part = panel[(i - k - 1) * b:(i - k) * b]
                hi = (i + 1) * b
                l_ref[i * b:hi, r0 + b:hi] = l_ref[i * b:hi, r0 + b:hi] - nt(part, panel[:(i - k) * b])
            l_ref[r0:r0 + b, r0 + b:] = jnp.zeros((b, l_ref.shape[1] - r0 - b), jnp.float32)
    last = blocks - 1
    tl = target - last * b
    lane8 = lax.broadcasted_iota(jnp.int32, (8, b), 1)
    row = l_ref[pl.ds(target, 1), :]
    zs = [None] * blocks
    for k in range(last, -1, -1):
        acc = jnp.broadcast_to(row[:, k * b:(k + 1) * b], (8, b))
        if k == last:
            acc = jnp.where(lane8 < tl, acc, 0.0)
        for i in range(k + 1, blocks):
            acc = acc - nn(zs[i], l_ref[i * b:(i + 1) * b, k * b:(k + 1) * b])
        zk = nn(acc, inverses[k])
        if k == last:
            zk = jnp.where(lane8 < tl, zk, 0.0)
        zs[k] = zk
        z_ref[:, k * b:(k + 1) * b] = zk


def cholesky_and_solve(sym, target, blocks):
    n = blocks * BLOCK
    last_steps = target + 1 - (blocks - 1) * BLOCK
    kernel = functools.partial(chol_kernel, blocks=blocks, last_steps=last_steps, target=target)
    vmem = pltpu.VMEM
    return pl.pallas_call(
        kernel,
        out_shape=(jax.ShapeDtypeStruct((n, n), jnp.float32), jax.ShapeDtypeStruct((8, n), jnp.float32)),
        in_specs=[pl.BlockSpec(memory_space=vmem)],
        out_specs=(pl.BlockSpec(memory_space=vmem), pl.BlockSpec(memory_space=vmem)),
        scratch_shapes=[pltpu.VMEM((BLOCK, BLOCK), jnp.float32)] * 3,
    )(sym)


def butterfly_sum(flat, axis, order):
    size = lax.axis_size(axis)
    steps = size.bit_length() - 1
    me = lax.axis_index(axis)
    current = flat
    for bit in order:
        half = current.shape[0] // 2
        low, high = current[:half], current[half:]
        upper_half = ((me >> bit) & 1) == 1
        send = jnp.where(upper_half, low, high)
        keep = jnp.where(upper_half, high, low)
        pairs = [(i, i ^ (1 << bit)) for i in range(size)]
        current = keep + lax.ppermute(send, axis, pairs)
    for bit in reversed(order):
        pairs = [(i, i ^ (1 << bit)) for i in range(size)]
        got = lax.ppermute(current, axis, pairs)
        upper_half = ((me >> bit) & 1) == 1
        current = jnp.where(
            upper_half, jnp.concatenate([got, current]), jnp.concatenate([current, got])
        )
    return current


def shards(features, labels, other_predictor, coefficients, panel_block):
    window, rows_here = features.shape
    row_devices = lax.axis_size("row")
    assert row_devices & (row_devices - 1) == 0
    total_rows = rows_here * row_devices
    first_col = panel_block[0] * PB
    window_coef = lax.dynamic_slice(coefficients, (first_col,), (window,))
    as_float = features.astype(jnp.float32)
    linear = jnp.dot(window_coef, as_float, precision=precise) + other_predictor
    fitted = jax.nn.sigmoid(linear)
    weight = jnp.maximum(fitted * (1.0 - fitted), 0.01)
    root_weight = jnp.sqrt(weight)
    norm_scale = 1.0 / math.sqrt(total_rows)
    scaled = as_float * (root_weight * norm_scale)[None, :]
    target = (
        root_weight * linear + (labels.astype(jnp.float32) - fitted) / root_weight
    ) * norm_scale
    working = jnp.concatenate([scaled, target[None, :]], axis=0)
    width = window + 1
    blocks = -(-width // BLOCK)
    size = blocks * BLOCK
    working = jnp.concatenate([working, jnp.zeros((size - width, rows_here), jnp.float32)], axis=0)
    local_gram = lax.dot_general(
        working, working, (((1,), (1,)), ((), ())), precision=precise
    )
    pieces = [
        local_gram[i * BLOCK:(i + 1) * BLOCK, k * BLOCK:(k + 1) * BLOCK]
        for i in range(blocks)
        for k in range(i + 1)
    ]
    used = len(pieces) * BLOCK
    quantum = row_devices * 8
    padded = -(-used // quantum) * quantum
    if padded > used:
        pieces.append(jnp.zeros((padded - used, BLOCK), jnp.float32))
    stacked = jnp.concatenate(pieces, axis=0)
    steps = row_devices.bit_length() - 1
    first = list(range(steps))
    second = [0, 2, 1] + first[3:] if steps >= 3 else first
    half = padded // 2
    packed = jnp.concatenate(
        [butterfly_sum(stacked[:half], "row", first), butterfly_sum(stacked[half:], "row", second)], axis=0
    )
    lower, solved = cholesky_and_solve(packed, window, blocks)
    lower_window = lower[:window, :window]
    coef = solved[0, :window]
    fitted_part = jnp.dot(coef, scaled, precision=precise)
    residual = (target - fitted_part) * math.sqrt(total_rows)
    return lower_window.T, residual


def solution(mesh):
    in_specs = (
        P(None, ("groups", "row")),
        P(("groups", "row")),
        P(("groups", "row")),
        P("groups"),
        P("groups"),
    )
    out_specs = (P("groups", None), P(("groups", "row")))
    return jax.shard_map(shards, mesh=mesh, in_specs=in_specs, out_specs=out_specs, check_vma=False)
```
